256 devices in a mesh: sample: 32 (over z, y_hi, core), tensor: 8 (over y_lo, x).
Axes of the slice: x: 4, y: 4 (y_hi: 2, y_lo: 2; y = y_hi * 2 + y_lo), z: 8, core: 2. Of those that a mesh axis runs over, the one named last changes fastest.
Arguments:
- hidden: bfloat16 [8192, 14336], P('sample', 'tensor'), may hold values from -6 to 6
- down_weight: bfloat16 [4096, 14336], P('sample', 'tensor'), may hold values from -0.046875 to 0.046875
- cotangent: bfloat16 [8192, 4096], P('sample'), may hold values from -6 to 6
- scores: int32 [128], P('sample'), may hold values from 0 to 38654
- prompt_ids: int32 [128], P('sample'), may hold values from 0 to 3, as said below
Outputs:
- layer_out: bfloat16 [8192, 4096], P('sample', 'tensor')
- hidden_grad: bfloat16 [8192, 14336], P('sample', 'tensor')
- weight_grad: bfloat16 [4096, 14336], P('sample', 'tensor')
The draws below stay inside these ranges and needn't reach their ends.
Inputs may be any that keep to these rules, and one draw needn't show every extreme that they name: `prompt_ids`: each prompt id names exactly 32 responses.
All inputs are finite; a program needn't handle non-finite values.
Results may differ from the reference program's by a relative error of at most 0.015.
Values may be sent and summed in bfloat16 or wider, within the bound.
No kernel may reach another device: no remote copies, remote signals or barrier semaphores. Data moves between devices by JAX's collectives and lax.ppermute only.
A program may use at most 128 MiB of HBM per device.

```python
import math
import jax
import jax.numpy as jnp
from jax import lax

D = 4096
FF = 14336
LEN = 64
GROUP = 32
TOK_DEV = 256
SAMPLES = 128
PROMPTS = 4
TOKENS = 8192
N_SAMPLE = 32
N_TENSOR = 8


def prompt_order(key):
    return jax.random.permutation(jax.random.fold_in(key, 7), SAMPLES).astype(jnp.int32)


def draw_prompt_ids(key, part):
    return (prompt_order(key) // GROUP).astype(jnp.int32)


def draw_scores(key, part):
    order = prompt_order(key)
    groups = (order // GROUP).astype(jnp.int32)
    ranks = (order % GROUP).astype(jnp.int32)
    offsets = jax.random.randint(jax.random.fold_in(key, 11), (PROMPTS,), 0, 64).astype(jnp.int32)
    onehot = (groups[:, None] == jnp.arange(PROMPTS, dtype=jnp.int32)[None, :]).astype(jnp.int32)
    base = groups * 12800 + jnp.sum(onehot * offsets[None, :], axis=1)
    noise = jax.random.randint(jax.random.fold_in(key, 13), (SAMPLES,), 0, 65).astype(jnp.int32)
    rising = 128 * jnp.arange(SAMPLES, dtype=jnp.int32) // SAMPLES
    raw = base + noise + rising
    lowest = (groups == 0) & (ranks == 0)
    highest = (groups == PROMPTS - 1) & (ranks == 1)
    top_value = jnp.int32((PROMPTS - 1) * 12800 + 254)
    raw = jnp.where(lowest, jnp.int32(0), jnp.where(highest, top_value, raw))
    return raw.astype(jnp.int32)


def raised(drawn, own_key, source, target, parts, factor):
    def block_of(axis_at):
        return (jnp.arange(drawn.shape[axis_at]) // (drawn.shape[axis_at] // parts)).reshape((-1,) + (1,) * (drawn.ndim - 1 - axis_at))

    one_side = jax.random.permutation(own_key, parts)[block_of(target)]
    far = (block_of(target) + parts // 2) % parts
    return jnp.where((block_of(source) == one_side) | (block_of(source) == far), factor * drawn, drawn)


def block_scale(own_key, shape, cuts, smallest, largest):
    def one(position, parts):
        draws = jax.random.uniform(jax.random.fold_in(jax.random.fold_in(own_key, 6), position), (parts,), jnp.float32, smallest / len(cuts), largest / len(cuts))
        return jnp.repeat(jnp.exp(draws), shape[position] // parts).reshape((-1,) + (1,) * (len(shape) - position - 1))

    gain = one(*cuts[0])
    for cut in cuts[1:]:
        gain = gain * one(*cut)
    return gain


def gaussian(stream_key, extent, scale, reach, shards=(), held_as=jnp.bfloat16):
    drawn = scale * jax.random.normal(stream_key, extent, jnp.float32)
    if shards:
        drawn = drawn * block_scale(stream_key, extent, shards, -0.22, 0.18)
    return jnp.clip(drawn, -reach, reach).astype(held_as)


def gaussian_with(rng, dims, spread, reach, pieces, heavy, held_as=jnp.bfloat16):
    result = spread * jax.random.normal(rng, dims, jnp.float32)
    if pieces:
        result = result * block_scale(rng, dims, pieces, -0.22, 0.18)
    return jnp.clip(raised(result, jax.random.fold_in(rng, 3), *heavy), -reach, reach).astype(held_as)


def setup_inputs(seed: int = 0) -> dict:
    key_list = jax.random.split(jax.random.key(seed), 6)
    return {
        "hidden": gaussian(key_list[0], (TOKENS, FF), 1.0, 6.0, ((0, 32), (1, 8))),
        "down_weight": gaussian(key_list[1], (D, FF), FF ** -0.5, 0.046875, ((0, 32), (1, 8))),
        "cotangent": gaussian_with(key_list[2], (TOKENS, D), 1.0, 6.0, ((0, 32),), (0, 1, 32, 2.75)),
        "scores": draw_scores(jax.random.fold_in(key_list[5], 71), 0),
        "prompt_ids": draw_prompt_ids(jax.random.fold_in(key_list[5], 71), 0),
    }


def reference(hidden, down_weight, cotangent, scores, prompt_ids):
    rewards = scores.astype(jnp.float32) / 64.0
    onehot = prompt_ids[:, None] == jnp.arange(PROMPTS, dtype=jnp.int32)[None, :]
    peak = lax.optimization_barrier(jnp.max(jnp.where(onehot, rewards[:, None], jnp.float32(-1e+30)), axis=0))
    total = lax.optimization_barrier(jnp.sum(jnp.where(onehot, jnp.exp(rewards[:, None] - peak[None, :]), jnp.float32(0.0)), axis=0))
    log_norm = peak + jnp.log(total)
    sample_norm = lax.optimization_barrier(jnp.sum(jnp.where(onehot, log_norm[None, :], jnp.float32(0.0)), axis=1))
    token_weight = jnp.repeat(GROUP * jnp.exp(rewards - sample_norm), LEN)
    weighted = (cotangent.astype(jnp.float32) * token_weight[:, None]).astype(jnp.bfloat16)
    block_ff = FF // N_TENSOR
    hid_blocks = hidden.reshape(TOKENS, N_TENSOR, block_ff).transpose(1, 0, 2)
    wgt_blocks = down_weight.reshape(D, N_TENSOR, block_ff).transpose(1, 0, 2)

    def add_out(acc, pair):
        part = lax.dot_general(pair[0], pair[1], (((1,), (1,)), ((), ())), preferred_element_type=jnp.float32)
        part = lax.optimization_barrier(part.astype(jnp.bfloat16))
        return (acc + part.astype(jnp.float32), None)
    out_acc, _ = lax.scan(add_out, jnp.zeros((TOKENS, D), jnp.float32), (hid_blocks, wgt_blocks))
    layer_out = out_acc.astype(jnp.bfloat16)
    hidden_grad = jnp.dot(weighted, down_weight, preferred_element_type=jnp.float32).astype(jnp.bfloat16)
    scale = 1.0 / math.sqrt(TOKENS)

    def add_grad(acc, pair):
        term = lax.dot_general(pair[0], pair[1], (((0,), (0,)), ((), ())), preferred_element_type=jnp.float32) * scale
        term = lax.optimization_barrier(term.astype(jnp.bfloat16))
        return (acc + term.astype(jnp.float32), None)
    grad_acc, _ = lax.scan(add_grad, jnp.zeros((D, FF), jnp.float32), (weighted.reshape(N_SAMPLE, TOK_DEV, D), hidden.reshape(N_SAMPLE, TOK_DEV, FF)))
    weight_grad = grad_acc.astype(jnp.bfloat16)
    return (layer_out, hidden_grad, weight_grad)
```

```python
import math

import jax
import jax.numpy as jnp
from jax import lax
from jax.sharding import Mesh
from jax.sharding import PartitionSpec as P

GROUP = 32
SAMPLE = ("z", "yhi", "core")
CHIPS = ("z", "yhi")


def shards(hidden, down_weight, cotangent, scores, prompt_ids):
    samples_here = scores.shape[0]
    n_sample = lax.axis_size(SAMPLE)
    n_core = lax.axis_size("core")
    n_chip = n_sample // n_core
    prompts = samples_here * n_sample // GROUP

    packed = jnp.concatenate([scores, prompt_ids])[None, :]
    everything = lax.all_gather(packed, SAMPLE, axis=0, tiled=True)
    all_scores = everything[:, :samples_here].reshape(-1)
    all_ids = everything[:, samples_here:].reshape(-1)
    all_rewards = all_scores.astype(jnp.float32) / 64.0
    all_onehot = all_ids[:, None] == jnp.arange(prompts, dtype=jnp.int32)[None, :]
    peak = jnp.max(jnp.where(all_onehot, all_rewards[:, None], jnp.float32(-1e30)), axis=0)
    shifted = jnp.where(all_onehot, jnp.exp(all_rewards[:, None] - peak[None, :]), 0.0)
    total = jnp.sum(shifted, axis=0)
    log_norm = peak + jnp.log(total)

    rewards = scores.astype(jnp.float32) / 64.0
    onehot = prompt_ids[:, None] == jnp.arange(prompts, dtype=jnp.int32)[None, :]
    sample_norm = jnp.sum(jnp.where(onehot, log_norm[None, :], 0.0), axis=1)
    tokens_here = hidden.shape[0]
    token_weight = jnp.repeat(GROUP * jnp.exp(rewards - sample_norm), tokens_here // samples_here)
    weighted = (cotangent.astype(jnp.float32) * token_weight[:, None]).astype(jnp.bfloat16)

    rows_w = down_weight.shape[0]
    d_all = weighted.shape[1]
    weighted_p = (
        weighted.reshape(tokens_here, n_chip, n_core, rows_w)
        .transpose(0, 2, 1, 3)
        .reshape(tokens_here, d_all)
    )
    gathered = lax.all_gather(down_weight, CHIPS, axis=0, tiled=True)
    gathered = lax.all_gather(gathered, "core", axis=0, tiled=True)

    partial_value = lax.dot_general(
        hidden, gathered, (((1,), (1,)), ((), ())), preferred_element_type=jnp.float32
    ).astype(jnp.bfloat16)
    partial_value = (
        partial_value.reshape(tokens_here, n_core, n_chip, rows_w)
        .transpose(0, 2, 1, 3)
        .reshape(tokens_here, d_all)
    )
    hidden_grad = jnp.dot(weighted_p, gathered, preferred_element_type=jnp.float32).astype(
        jnp.bfloat16
    )
    layer_out = lax.psum_scatter(partial_value, "tensor", scatter_dimension=1, tiled=True)
    scale = 1.0 / math.sqrt(tokens_here * n_sample)
    grad_part = (
        lax.dot_general(
            weighted_p, hidden, (((0,), (0,)), ((), ())), preferred_element_type=jnp.float32
        )
        * scale
    ).astype(jnp.bfloat16)
    grad_part = lax.psum_scatter(grad_part, "core", scatter_dimension=0, tiled=True)
    weight_grad = lax.psum_scatter(grad_part, CHIPS, scatter_dimension=0, tiled=True)
    return (layer_out, hidden_grad, weight_grad)


def solution(mesh):
    n_tensor = mesh.shape["tensor"]
    fine = Mesh(mesh.devices.reshape(-1, 2, 2, n_tensor), ("z", "yhi", "core", "tensor"))
    return jax.shard_map(
        shards,
        mesh=fine,
        in_specs=(
            P(SAMPLE, "tensor"),
            P(SAMPLE, "tensor"),
            P(SAMPLE, None),
            P(SAMPLE),
            P(SAMPLE),
        ),
        out_specs=(P(SAMPLE, "tensor"), P(SAMPLE, "tensor"), P(SAMPLE, "tensor")),
        check_vma=False,
    )
```

```python
import math

import jax
import jax.numpy as jnp
from jax import lax
from jax.sharding import PartitionSpec as P

GROUP = 32


def sum_to_bf16(received, axis):
    return jnp.sum(received.astype(jnp.float32), axis=axis).astype(jnp.bfloat16)


def shards(hidden, down_weight, cotangent, scores, prompt_ids):
    samples_here = scores.shape[0]
    n_sample = lax.axis_size("sample")
    n_tensor = lax.axis_size("tensor")
    prompts = samples_here * n_sample // GROUP

    packed = jnp.concatenate([scores, prompt_ids])[None, :]
    everything = lax.all_gather(packed, "sample", axis=0, tiled=True)
    all_scores = everything[:, :samples_here].reshape(-1)
    all_ids = everything[:, samples_here:].reshape(-1)
    all_rewards = all_scores.astype(jnp.float32) / 64.0
    all_onehot = all_ids[:, None] == jnp.arange(prompts, dtype=jnp.int32)[None, :]
    peak = jnp.max(jnp.where(all_onehot, all_rewards[:, None], jnp.float32(-1e30)), axis=0)
    shifted = jnp.where(all_onehot, jnp.exp(all_rewards[:, None] - peak[None, :]), 0.0)
    total = jnp.sum(shifted, axis=0)
    log_norm = peak + jnp.log(total)

    rewards = scores.astype(jnp.float32) / 64.0
    onehot = prompt_ids[:, None] == jnp.arange(prompts, dtype=jnp.int32)[None, :]
    sample_norm = jnp.sum(jnp.where(onehot, log_norm[None, :], 0.0), axis=1)
    tokens_here = hidden.shape[0]
    token_weight = jnp.repeat(GROUP * jnp.exp(rewards - sample_norm), tokens_here // samples_here)
    weighted = (cotangent.astype(jnp.float32) * token_weight[:, None]).astype(jnp.bfloat16)

    ff_here = hidden.shape[1]
    cut = ff_here // 2
    scale = 1.0 / math.sqrt(tokens_here * n_sample)

    def grad_term(cols):
        return (
            lax.dot_general(
                weighted, cols, (((0,), (0,)), ((), ())), preferred_element_type=jnp.float32
            )
            * scale
        ).astype(jnp.bfloat16)

    grad_a = lax.psum_scatter(grad_term(hidden[:, :cut]), "sample", scatter_dimension=0, tiled=True)
    term_b = grad_term(hidden[:, cut:])
    rows_here = down_weight.shape[0]
    term_b = term_b.reshape(n_sample, rows_here, ff_here - cut)
    grad_b = sum_to_bf16(lax.all_to_all(term_b, "sample", 0, 0, tiled=True), 0)
    weight_grad = jnp.concatenate([grad_a, grad_b], axis=1)

    gathered = lax.all_gather(down_weight, "sample", axis=0, tiled=True)
    partial_value = lax.dot_general(
        hidden, gathered, (((1,), (1,)), ((), ())), preferred_element_type=jnp.float32
    ).astype(jnp.bfloat16)
    d_all = partial_value.shape[1]
    partial_value = partial_value.reshape(tokens_here, n_tensor, d_all // n_tensor)
    layer_out = sum_to_bf16(lax.all_to_all(partial_value, "tensor", 1, 1, tiled=True), 1)
    hidden_grad = jnp.dot(weighted, gathered, preferred_element_type=jnp.float32).astype(
        jnp.bfloat16
    )
    return (layer_out, hidden_grad, weight_grad)


def solution(mesh):
    return jax.shard_map(
        shards,
        mesh=mesh,
        in_specs=(
            P("sample", "tensor"),
            P("sample", "tensor"),
            P("sample", None),
            P("sample"),
            P("sample"),
        ),
        out_specs=(P("sample", "tensor"), P("sample", "tensor"), P("sample", "tensor")),
        check_vma=False,
    )
```

```python
import math

import jax
import jax.numpy as jnp
from jax import lax
from jax.sharding import Mesh
from jax.sharding import PartitionSpec as P

GROUP = 32
SAMPLE = ("z", "yhi", "core")


def sum_to_bf16(received, axis):
    return jnp.sum(received.astype(jnp.float32), axis=axis).astype(jnp.bfloat16)


def shards(hidden, down_weight, cotangent, scores, prompt_ids):
    samples_here = scores.shape[0]
    n_sample = lax.axis_size(SAMPLE)
    n_z = lax.axis_size("z")
    n_yhi = lax.axis_size("yhi")
    n_core = lax.axis_size("core")
    n_tensor = lax.axis_size("tensor")
    prompts = samples_here * n_sample // GROUP

    packed = jnp.concatenate([scores, prompt_ids])[None, :]
    everything = lax.all_gather(packed, SAMPLE, axis=0, tiled=True)
    all_scores = everything[:, :samples_here].reshape(-1)
    all_ids = everything[:, samples_here:].reshape(-1)
    all_rewards = all_scores.astype(jnp.float32) / 64.0
    all_onehot = all_ids[:, None] == jnp.arange(prompts, dtype=jnp.int32)[None, :]
    peak = jnp.max(jnp.where(all_onehot, all_rewards[:, None], jnp.float32(-1e30)), axis=0)
    shifted = jnp.where(all_onehot, jnp.exp(all_rewards[:, None] - peak[None, :]), 0.0)
    total = jnp.sum(shifted, axis=0)
    log_norm = peak + jnp.log(total)

    rewards = scores.astype(jnp.float32) / 64.0
    onehot = prompt_ids[:, None] == jnp.arange(prompts, dtype=jnp.int32)[None, :]
    sample_norm = jnp.sum(jnp.where(onehot, log_norm[None, :], 0.0), axis=1)
    tokens_here = hidden.shape[0]
    token_weight = jnp.repeat(GROUP * jnp.exp(rewards - sample_norm), tokens_here // samples_here)
    weighted = (cotangent.astype(jnp.float32) * token_weight[:, None]).astype(jnp.bfloat16)

    rows_w = down_weight.shape[0]
    d_all = weighted.shape[1]
    weighted_p = (
        weighted.reshape(tokens_here, n_z, n_yhi, n_core, rows_w)
        .transpose(0, 3, 2, 1, 4)
        .reshape(tokens_here, d_all)
    )
    gathered = lax.all_gather(down_weight, "z", axis=0, tiled=True)
    gathered = lax.all_gather(gathered, "yhi", axis=0, tiled=True)
    gathered = lax.all_gather(gathered, "core", axis=0, tiled=True)

    scale = 1.0 / math.sqrt(tokens_here * n_sample)
    grad_part = (
        lax.dot_general(
            weighted_p, hidden, (((0,), (0,)), ((), ())), preferred_element_type=jnp.float32
        )
        * scale
    ).astype(jnp.bfloat16)
    grad_part = lax.psum_scatter(grad_part, "core", scatter_dimension=0, tiled=True)
    grad_part = lax.psum_scatter(grad_part, "yhi", scatter_dimension=0, tiled=True)
    weight_grad = lax.psum_scatter(grad_part, "z", scatter_dimension=0, tiled=True)

    partial_value = lax.dot_general(
        hidden, gathered, (((1,), (1,)), ((), ())), preferred_element_type=jnp.float32
    ).astype(jnp.bfloat16)
    partial_value = (
        partial_value.reshape(tokens_here, n_core, n_yhi, n_z, rows_w)
        .transpose(0, 3, 2, 1, 4)
        .reshape(tokens_here, n_tensor, d_all // n_tensor)
    )
    layer_out = sum_to_bf16(lax.all_to_all(partial_value, "tensor", 1, 1, tiled=True), 1)
    hidden_grad = jnp.dot(weighted_p, gathered, preferred_element_type=jnp.float32).astype(
        jnp.bfloat16
    )
    return (layer_out, hidden_grad, weight_grad)


def solution(mesh):
    n_tensor = mesh.shape["tensor"]
    fine = Mesh(mesh.devices.reshape(-1, 2, 2, n_tensor), ("z", "yhi", "core", "tensor"))
    return jax.shard_map(
        shards,
        mesh=fine,
        in_specs=(
            P(SAMPLE, "tensor"),
            P(SAMPLE, "tensor"),
            P(SAMPLE, None),
            P(SAMPLE),
            P(SAMPLE),
        ),
        out_specs=(P(SAMPLE, "tensor"), P(SAMPLE, "tensor"), P(SAMPLE, "tensor")),
        check_vma=False,
    )
```

```python
import math

import jax
import jax.numpy as jnp
from jax import lax
from jax.sharding import Mesh
from jax.sharding import PartitionSpec as P

GROUP = 32
SAMPLE = ("z", "yhi", "core")


def sum_to_bf16(received, axis):
    return jnp.sum(received.astype(jnp.float32), axis=axis).astype(jnp.bfloat16)


def shards(hidden, down_weight, cotangent, scores, prompt_ids):
    samples_here = scores.shape[0]
    n_sample = lax.axis_size(SAMPLE)
    n_z = lax.axis_size("z")
    n_yhi = lax.axis_size("yhi")
    n_core = lax.axis_size("core")
    n_tensor = lax.axis_size("tensor")
    prompts = samples_here * n_sample // GROUP

    packed = jnp.concatenate([scores, prompt_ids])[None, :]
    everything = lax.all_gather(packed, SAMPLE, axis=0, tiled=True)
    all_scores = everything[:, :samples_here].reshape(-1)
    all_ids = everything[:, samples_here:].reshape(-1)
    all_rewards = all_scores.astype(jnp.float32) / 64.0
    all_onehot = all_ids[:, None] == jnp.arange(prompts, dtype=jnp.int32)[None, :]
    peak = jnp.max(jnp.where(all_onehot, all_rewards[:, None], jnp.float32(-1e30)), axis=0)
    shifted = jnp.where(all_onehot, jnp.exp(all_rewards[:, None] - peak[None, :]), 0.0)
    total = jnp.sum(shifted, axis=0)
    log_norm = peak + jnp.log(total)

    rewards = scores.astype(jnp.float32) / 64.0
    onehot = prompt_ids[:, None] == jnp.arange(prompts, dtype=jnp.int32)[None, :]
    sample_norm = jnp.sum(jnp.where(onehot, log_norm[None, :], 0.0), axis=1)
    tokens_here = hidden.shape[0]
    token_weight = jnp.repeat(GROUP * jnp.exp(rewards - sample_norm), tokens_here // samples_here)
    weighted = (cotangent.astype(jnp.float32) * token_weight[:, None]).astype(jnp.bfloat16)

    rows_w = down_weight.shape[0]
    d_all = weighted.shape[1]
    own_first = lax.axis_index("yhi") == 0
    weighted_5 = weighted.reshape(tokens_here, n_z, n_yhi, n_core, rows_w)
    weighted_p = (
        jnp.where(own_first, weighted_5, jnp.flip(weighted_5, axis=2))
        .transpose(0, 3, 2, 1, 4)
        .reshape(tokens_here, d_all)
    )
    swap = [(0, 1), (1, 0)]
    gathered = lax.all_gather(down_weight, "z", axis=0, tiled=True)
    gathered = jnp.concatenate([gathered, lax.ppermute(gathered, "yhi", swap)], axis=0)
    gathered = lax.all_gather(gathered, "core", axis=0, tiled=True)

    scale = 1.0 / math.sqrt(tokens_here * n_sample)
    grad_part = (
        lax.dot_general(
            weighted_p, hidden, (((0,), (0,)), ((), ())), preferred_element_type=jnp.float32
        )
        * scale
    ).astype(jnp.bfloat16)
    grad_part = lax.psum_scatter(grad_part, "core", scatter_dimension=0, tiled=True)
    half = grad_part.shape[0] // n_yhi
    grad_part = (
        grad_part[:half].astype(jnp.float32)
        + lax.ppermute(grad_part[half:], "yhi", swap).astype(jnp.float32)
    ).astype(jnp.bfloat16)
    weight_grad = lax.psum_scatter(grad_part, "z", scatter_dimension=0, tiled=True)

    partial_value = lax.dot_general(
        hidden, gathered, (((1,), (1,)), ((), ())), preferred_element_type=jnp.float32
    ).astype(jnp.bfloat16)
    partial_value = partial_value.reshape(tokens_here, n_core, n_yhi, n_z, rows_w).transpose(
        0, 3, 2, 1, 4
    )
    partial_value = jnp.where(own_first, partial_value, jnp.flip(partial_value, axis=2)).reshape(
        tokens_here, n_tensor, d_all // n_tensor
    )
    layer_out = sum_to_bf16(lax.all_to_all(partial_value, "tensor", 1, 1, tiled=True), 1)
    hidden_grad = jnp.dot(weighted_p, gathered, preferred_element_type=jnp.float32).astype(
        jnp.bfloat16
    )
    return (layer_out, hidden_grad, weight_grad)


def solution(mesh):
    n_tensor = mesh.shape["tensor"]
    fine = Mesh(mesh.devices.reshape(-1, 2, 2, n_tensor), ("z", "yhi", "core", "tensor"))
    return jax.shard_map(
        shards,
        mesh=fine,
        in_specs=(
            P(SAMPLE, "tensor"),
            P(SAMPLE, "tensor"),
            P(SAMPLE, None),
            P(SAMPLE),
            P(SAMPLE),
        ),
        out_specs=(P(SAMPLE, "tensor"), P(SAMPLE, "tensor"), P(SAMPLE, "tensor")),
        check_vma=False,
    )
```

```python
import math

import jax
import jax.numpy as jnp
from jax import lax
from jax.sharding import Mesh
from jax.sharding import PartitionSpec as P

GROUP = 32
SAMPLE = ("z", "yhi", "core")


def sum_to_bf16(received, axis):
    return jnp.sum(received.astype(jnp.float32), axis=axis).astype(jnp.bfloat16)


def shards(hidden, down_weight, cotangent, scores, prompt_ids):
    samples_here = scores.shape[0]
    n_sample = lax.axis_size(SAMPLE)
    n_z = lax.axis_size("z")
    n_yhi = lax.axis_size("yhi")
    n_core = lax.axis_size("core")
    n_tensor = lax.axis_size("tensor")
    prompts = samples_here * n_sample // GROUP

    packed = jnp.concatenate([scores, prompt_ids])[None, :]
    everything = lax.all_gather(packed, SAMPLE, axis=0, tiled=True)
    all_scores = everything[:, :samples_here].reshape(-1)
    all_ids = everything[:, samples_here:].reshape(-1)
    all_rewards = all_scores.astype(jnp.float32) / 64.0
    all_onehot = all_ids[:, None] == jnp.arange(prompts, dtype=jnp.int32)[None, :]
    peak = jnp.max(jnp.where(all_onehot, all_rewards[:, None], jnp.float32(-1e30)), axis=0)
    shifted = jnp.where(all_onehot, jnp.exp(all_rewards[:, None] - peak[None, :]), 0.0)
    total = jnp.sum(shifted, axis=0)
    log_norm = peak + jnp.log(total)

    rewards = scores.astype(jnp.float32) / 64.0
    onehot = prompt_ids[:, None] == jnp.arange(prompts, dtype=jnp.int32)[None, :]
    sample_norm = jnp.sum(jnp.where(onehot, log_norm[None, :], 0.0), axis=1)
    tokens_here = hidden.shape[0]
    token_weight = jnp.repeat(GROUP * jnp.exp(rewards - sample_norm), tokens_here // samples_here)
    weighted = (cotangent.astype(jnp.float32) * token_weight[:, None]).astype(jnp.bfloat16)

    rows_w = down_weight.shape[0]
    d_all = weighted.shape[1]
    own_first = lax.axis_index("yhi") == 0
    weighted_5 = weighted.reshape(tokens_here, n_z, n_yhi, n_core, rows_w)
    weighted_p = (
        jnp.where(own_first, weighted_5, jnp.flip(weighted_5, axis=2))
        .transpose(0, 3, 1, 2, 4)
        .reshape(tokens_here, d_all)
    )
    swap = [(0, 1), (1, 0)]
    gathered = jnp.concatenate([down_weight, lax.ppermute(down_weight, "yhi", swap)], axis=0)
    gathered = lax.all_gather(gathered, "z", axis=0, tiled=True)
    gathered = lax.all_gather(gathered, "core", axis=0, tiled=True)

    scale = 1.0 / math.sqrt(tokens_here * n_sample)
    grad_part = (
        lax.dot_general(
            weighted_p, hidden, (((0,), (0,)), ((), ())), preferred_element_type=jnp.float32
        )
        * scale
    ).astype(jnp.bfloat16)
    grad_part = lax.psum_scatter(grad_part, "core", scatter_dimension=0, tiled=True)
    grad_part = lax.psum_scatter(grad_part, "z", scatter_dimension=0, tiled=True)
    weight_grad = (
        grad_part[:rows_w].astype(jnp.float32)
        + lax.ppermute(grad_part[rows_w:], "yhi", swap).astype(jnp.float32)
    ).astype(jnp.bfloat16)

    partial_value = lax.dot_general(
        hidden, gathered, (((1,), (1,)), ((), ())), preferred_element_type=jnp.float32
    ).astype(jnp.bfloat16)
    partial_value = partial_value.reshape(tokens_here, n_core, n_z, n_yhi, rows_w).transpose(
        0, 2, 3, 1, 4
    )
    partial_value = jnp.where(own_first, partial_value, jnp.flip(partial_value, axis=2)).reshape(
        tokens_here, n_tensor, d_all // n_tensor
    )
    layer_out = sum_to_bf16(lax.all_to_all(partial_value, "tensor", 1, 1, tiled=True), 1)
    hidden_grad = jnp.dot(weighted_p, gathered, preferred_element_type=jnp.float32).astype(
        jnp.bfloat16
    )
    return (layer_out, hidden_grad, weight_grad)


def solution(mesh):
    n_tensor = mesh.shape["tensor"]
    fine = Mesh(mesh.devices.reshape(-1, 2, 2, n_tensor), ("z", "yhi", "core", "tensor"))
    return jax.shard_map(
        shards,
        mesh=fine,
        in_specs=(
            P(SAMPLE, "tensor"),
            P(SAMPLE, "tensor"),
            P(SAMPLE, None),
            P(SAMPLE),
            P(SAMPLE),
        ),
        out_specs=(P(SAMPLE, "tensor"), P(SAMPLE, "tensor"), P(SAMPLE, "tensor")),
        check_vma=False,
    )
```

```python
import math

import jax
import jax.numpy as jnp
from jax import lax
from jax.sharding import Mesh
from jax.sharding import PartitionSpec as P

GROUP = 32
SAMPLE = ("z", "yhi", "core")


def sum_to_bf16(received, axis):
    return jnp.sum(received.astype(jnp.float32), axis=axis).astype(jnp.bfloat16)


def shards(hidden, down_weight, cotangent, scores, prompt_ids):
    samples_here = scores.shape[0]
    n_sample = lax.axis_size(SAMPLE)
    n_z = lax.axis_size("z")
    n_yhi = lax.axis_size("yhi")
    n_core = lax.axis_size("core")
    n_tensor = lax.axis_size("tensor")
    prompts = samples_here * n_sample // GROUP

    packed = jnp.concatenate([scores, prompt_ids])[None, :]
    everything = lax.all_gather(packed, SAMPLE, axis=0, tiled=True)
    all_scores = everything[:, :samples_here].reshape(-1)
    all_ids = everything[:, samples_here:].reshape(-1)
    all_rewards = all_scores.astype(jnp.float32) / 64.0
    all_onehot = all_ids[:, None] == jnp.arange(prompts, dtype=jnp.int32)[None, :]
    peak = jnp.max(jnp.where(all_onehot, all_rewards[:, None], jnp.float32(-1e30)), axis=0)
    shifted = jnp.where(all_onehot, jnp.exp(all_rewards[:, None] - peak[None, :]), 0.0)
    total = jnp.sum(shifted, axis=0)
    log_norm = peak + jnp.log(total)

    rewards = scores.astype(jnp.float32) / 64.0
    onehot = prompt_ids[:, None] == jnp.arange(prompts, dtype=jnp.int32)[None, :]
    sample_norm = jnp.sum(jnp.where(onehot, log_norm[None, :], 0.0), axis=1)
    tokens_here = hidden.shape[0]
    token_weight = jnp.repeat(GROUP * jnp.exp(rewards - sample_norm), tokens_here // samples_here)
    weighted = (cotangent.astype(jnp.float32) * token_weight[:, None]).astype(jnp.bfloat16)

    rows_w = down_weight.shape[0]
    d_all = weighted.shape[1]
    ff_here = hidden.shape[1]
    cut = ff_here // 2
    swap = [(0, 1), (1, 0)]
    own_first = lax.axis_index("yhi") == 0
    weighted_5 = weighted.reshape(tokens_here, n_z, n_yhi, n_core, rows_w)
    weighted_rel = jnp.where(own_first, weighted_5, jnp.flip(weighted_5, axis=2))
    weighted_a = weighted_rel.transpose(0, 3, 2, 1, 4).reshape(tokens_here, d_all)
    weighted_b = weighted_rel.transpose(0, 3, 1, 2, 4).reshape(tokens_here, d_all)

    gathered_a = lax.all_gather(down_weight[:, :cut], "z", axis=0, tiled=True)
    gathered_a = jnp.concatenate([gathered_a, lax.ppermute(gathered_a, "yhi", swap)], axis=0)
    gathered_a = lax.all_gather(gathered_a, "core", axis=0, tiled=True)
    weight_b = down_weight[:, cut:]
    gathered_b = jnp.concatenate([weight_b, lax.ppermute(weight_b, "yhi", swap)], axis=0)
    gathered_b = lax.all_gather(gathered_b, "z", axis=0, tiled=True)
    gathered_b = lax.all_gather(gathered_b, "core", axis=0, tiled=True)

    scale = 1.0 / math.sqrt(tokens_here * n_sample)

    def grad_term(rows, cols):
        return (
            lax.dot_general(rows, cols, (((0,), (0,)), ((), ())), preferred_element_type=jnp.float32)
            * scale
        ).astype(jnp.bfloat16)

    def add_swapped(mine, theirs):
        got = lax.ppermute(theirs, "yhi", swap)
        return (mine.astype(jnp.float32) + got.astype(jnp.float32)).astype(jnp.bfloat16)

    grad_a = grad_term(weighted_a, hidden[:, :cut])
    grad_a = lax.psum_scatter(grad_a, "core", scatter_dimension=0, tiled=True)
    half = grad_a.shape[0] // n_yhi
    grad_a = add_swapped(grad_a[:half], grad_a[half:])
    grad_a = lax.psum_scatter(grad_a, "z", scatter_dimension=0, tiled=True)
    grad_b = grad_term(weighted_b, hidden[:, cut:])
    grad_b = lax.psum_scatter(grad_b, "core", scatter_dimension=0, tiled=True)
    grad_b = lax.psum_scatter(grad_b, "z", scatter_dimension=0, tiled=True)
    grad_b = add_swapped(grad_b[:rows_w], grad_b[rows_w:])
    weight_grad = jnp.concatenate([grad_a, grad_b], axis=1)

    value_a = lax.dot_general(
        hidden[:, :cut], gathered_a, (((1,), (1,)), ((), ())), preferred_element_type=jnp.float32
    )
    value_b = lax.dot_general(
        hidden[:, cut:], gathered_b, (((1,), (1,)), ((), ())), preferred_element_type=jnp.float32
    )
    partial_value = value_a.reshape(tokens_here, n_core, n_yhi, n_z, rows_w).transpose(
        0, 3, 2, 1, 4
    ) + value_b.reshape(tokens_here, n_core, n_z, n_yhi, rows_w).transpose(0, 2, 3, 1, 4)
    partial_value = jnp.where(own_first, partial_value, jnp.flip(partial_value, axis=2))
    partial_value = partial_value.astype(jnp.bfloat16).reshape(
        tokens_here, n_tensor, d_all // n_tensor
    )
    layer_out = sum_to_bf16(lax.all_to_all(partial_value, "tensor", 1, 1, tiled=True), 1)
    hidden_grad = jnp.concatenate(
        [
            jnp.dot(weighted_a, gathered_a, preferred_element_type=jnp.float32),
            jnp.dot(weighted_b, gathered_b, preferred_element_type=jnp.float32),
        ],
        axis=1,
    ).astype(jnp.bfloat16)
    return (layer_out, hidden_grad, weight_grad)


def solution(mesh):
    n_tensor = mesh.shape["tensor"]
    fine = Mesh(mesh.devices.reshape(-1, 2, 2, n_tensor), ("z", "yhi", "core", "tensor"))
    return jax.shard_map(
        shards,
        mesh=fine,
        in_specs=(
            P(SAMPLE, "tensor"),
            P(SAMPLE, "tensor"),
            P(SAMPLE, None),
            P(SAMPLE),
            P(SAMPLE),
        ),
        out_specs=(P(SAMPLE, "tensor"), P(SAMPLE, "tensor"), P(SAMPLE, "tensor")),
        check_vma=False,
    )
```

```python
import math

import jax
import jax.numpy as jnp
from jax import lax
from jax.sharding import Mesh
from jax.sharding import PartitionSpec as P

GROUP = 32
SAMPLE = ("z", "yhi", "core")


def sum_to_bf16(received, axis):
    return jnp.sum(received.astype(jnp.float32), axis=axis).astype(jnp.bfloat16)


def ring_gather(x, axis, n):
    fwd = [(i, (i + 1) % n) for i in range(n)]
    bwd = [(i, (i - 1) % n) for i in range(n)]
    from_minus, from_plus = [], []
    m, p = x, x
    for _ in range(n // 2 - 1):
        m = lax.ppermute(m, axis, fwd)
        p = lax.ppermute(p, axis, bwd)
        from_minus.append(m)
        from_plus.append(p)
    h = x.shape[0] // 2
    far = jnp.concatenate([lax.ppermute(m[:h], axis, fwd), lax.ppermute(p[h:], axis, bwd)], axis=0)
    return jnp.concatenate([x, *from_plus, far, *from_minus[::-1]], axis=0)


def shards(hidden, down_weight, cotangent, scores, prompt_ids):
    samples_here = scores.shape[0]
    n_sample = lax.axis_size(SAMPLE)
    n_z = lax.axis_size("z")
    n_yhi = lax.axis_size("yhi")
    n_core = lax.axis_size("core")
    n_tensor = lax.axis_size("tensor")
    prompts = samples_here * n_sample // GROUP

    packed = jnp.concatenate([scores, prompt_ids])[None, :]
    everything = lax.all_gather(packed, SAMPLE, axis=0, tiled=True)
    all_scores = everything[:, :samples_here].reshape(-1)
    all_ids = everything[:, samples_here:].reshape(-1)
    all_rewards = all_scores.astype(jnp.float32) / 64.0
    all_onehot = all_ids[:, None] == jnp.arange(prompts, dtype=jnp.int32)[None, :]
    peak = jnp.max(jnp.where(all_onehot, all_rewards[:, None], jnp.float32(-1e30)), axis=0)
    shifted = jnp.where(all_onehot, jnp.exp(all_rewards[:, None] - peak[None, :]), 0.0)
    total = jnp.sum(shifted, axis=0)
    log_norm = peak + jnp.log(total)

    rewards = scores.astype(jnp.float32) / 64.0
    onehot = prompt_ids[:, None] == jnp.arange(prompts, dtype=jnp.int32)[None, :]
    sample_norm = jnp.sum(jnp.where(onehot, log_norm[None, :], 0.0), axis=1)
    tokens_here = hidden.shape[0]
    token_weight = jnp.repeat(GROUP * jnp.exp(rewards - sample_norm), tokens_here // samples_here)
    weighted = (cotangent.astype(jnp.float32) * token_weight[:, None]).astype(jnp.bfloat16)

    rows_w = down_weight.shape[0]
    d_all = weighted.shape[1]
    own_first = lax.axis_index("yhi") == 0
    weighted_5 = weighted.reshape(tokens_here, n_z, n_yhi, n_core, rows_w)
    weighted_rel = jnp.where(own_first, weighted_5, jnp.flip(weighted_5, axis=2))
    weighted_p = weighted_rel.transpose(0, 3, 1, 2, 4).reshape(tokens_here, d_all)
    my_z = lax.axis_index("z")
    weighted_g = (
        jnp.roll(weighted_rel, -my_z, axis=1).transpose(0, 3, 1, 2, 4).reshape(tokens_here, d_all)
    )
    swap = [(0, 1), (1, 0)]
    gathered = jnp.concatenate([down_weight, lax.ppermute(down_weight, "yhi", swap)], axis=0)
    gathered = ring_gather(gathered, "z", n_z)
    gathered = lax.all_gather(gathered, "core", axis=0, tiled=True)

    scale = 1.0 / math.sqrt(tokens_here * n_sample)
    grad_part = (
        lax.dot_general(
            weighted_p, hidden, (((0,), (0,)), ((), ())), preferred_element_type=jnp.float32
        )
        * scale
    ).astype(jnp.bfloat16)
    grad_part = lax.psum_scatter(grad_part, "core", scatter_dimension=0, tiled=True)
    grad_part = lax.psum_scatter(grad_part, "z", scatter_dimension=0, tiled=True)
    weight_grad = (
        grad_part[:rows_w].astype(jnp.float32)
        + lax.ppermute(grad_part[rows_w:], "yhi", swap).astype(jnp.float32)
    ).astype(jnp.bfloat16)

    partial_value = lax.dot_general(
        hidden, gathered, (((1,), (1,)), ((), ())), preferred_element_type=jnp.float32
    ).astype(jnp.bfloat16)
    partial_value = partial_value.reshape(tokens_here, n_core, n_z, n_yhi, rows_w).transpose(
        0, 2, 3, 1, 4
    )
    partial_value = jnp.roll(partial_value, my_z, axis=1)
    partial_value = jnp.where(own_first, partial_value, jnp.flip(partial_value, axis=2)).reshape(
        tokens_here, n_tensor, d_all // n_tensor
    )
    layer_out = sum_to_bf16(lax.all_to_all(partial_value, "tensor", 1, 1, tiled=True), 1)
    hidden_grad = jnp.dot(weighted_g, gathered, preferred_element_type=jnp.float32).astype(
        jnp.bfloat16
    )
    return (layer_out, hidden_grad, weight_grad)


def solution(mesh):
    n_tensor = mesh.shape["tensor"]
    fine = Mesh(mesh.devices.reshape(-1, 2, 2, n_tensor), ("z", "yhi", "core", "tensor"))
    return jax.shard_map(
        shards,
        mesh=fine,
        in_specs=(
            P(SAMPLE, "tensor"),
            P(SAMPLE, "tensor"),
            P(SAMPLE, None),
            P(SAMPLE),
            P(SAMPLE),
        ),
        out_specs=(P(SAMPLE, "tensor"), P(SAMPLE, "tensor"), P(SAMPLE, "tensor")),
        check_vma=False,
    )
```

```python
import math

import jax
import jax.numpy as jnp
from jax import lax
from jax.sharding import Mesh
from jax.sharding import PartitionSpec as P

GROUP = 32
SAMPLE = ("z", "yhi", "core")


def sum_to_bf16(received, axis):
    return jnp.sum(received.astype(jnp.float32), axis=axis).astype(jnp.bfloat16)


def shards(hidden, down_weight, cotangent, scores, prompt_ids):
    samples_here = scores.shape[0]
    n_sample = lax.axis_size(SAMPLE)
    n_z = lax.axis_size("z")
    n_yhi = lax.axis_size("yhi")
    n_core = lax.axis_size("core")
    n_tensor = lax.axis_size("tensor")
    prompts = samples_here * n_sample // GROUP

    packed = jnp.concatenate([scores, prompt_ids])[None, :]
    everything = lax.all_gather(packed, SAMPLE, axis=0, tiled=True)
    all_scores = everything[:, :samples_here].reshape(-1)
    all_ids = everything[:, samples_here:].reshape(-1)
    all_rewards = all_scores.astype(jnp.float32) / 64.0
    all_onehot = all_ids[:, None] == jnp.arange(prompts, dtype=jnp.int32)[None, :]
    peak = jnp.max(jnp.where(all_onehot, all_rewards[:, None], jnp.float32(-1e30)), axis=0)
    shifted = jnp.where(all_onehot, jnp.exp(all_rewards[:, None] - peak[None, :]), 0.0)
    total = jnp.sum(shifted, axis=0)
    log_norm = peak + jnp.log(total)

    rewards = scores.astype(jnp.float32) / 64.0
    onehot = prompt_ids[:, None] == jnp.arange(prompts, dtype=jnp.int32)[None, :]
    sample_norm = jnp.sum(jnp.where(onehot, log_norm[None, :], 0.0), axis=1)
    tokens_here = hidden.shape[0]
    token_weight = jnp.repeat(GROUP * jnp.exp(rewards - sample_norm), tokens_here // samples_here)
    weighted = (cotangent.astype(jnp.float32) * token_weight[:, None]).astype(jnp.bfloat16)

    rows_w = down_weight.shape[0]
    d_all = weighted.shape[1]
    own_first = lax.axis_index("yhi") == 0
    weighted_5 = weighted.reshape(tokens_here, n_z, n_yhi, n_core, rows_w)
    weighted_p = (
        jnp.where(own_first, weighted_5, jnp.flip(weighted_5, axis=2))
        .transpose(0, 3, 2, 1, 4)
        .reshape(tokens_here, d_all)
    )
    swap = [(0, 1), (1, 0)]
    gathered_own = lax.all_gather(down_weight, "z", axis=0, tiled=True)
    gathered_partner = lax.all_gather(
        lax.ppermute(down_weight, "yhi", swap), "z", axis=0, tiled=True
    )
    gathered = jnp.concatenate([gathered_own, gathered_partner], axis=0)
    gathered = lax.all_gather(gathered, "core", axis=0, tiled=True)

    scale = 1.0 / math.sqrt(tokens_here * n_sample)
    grad_part = (
        lax.dot_general(
            weighted_p, hidden, (((0,), (0,)), ((), ())), preferred_element_type=jnp.float32
        )
        * scale
    ).astype(jnp.bfloat16)
    grad_part = lax.psum_scatter(grad_part, "core", scatter_dimension=0, tiled=True)
    half = grad_part.shape[0] // n_yhi
    theirs = lax.psum_scatter(grad_part[half:], "z", scatter_dimension=0, tiled=True)
    mine = lax.psum_scatter(grad_part[:half], "z", scatter_dimension=0, tiled=True)
    weight_grad = (
        mine.astype(jnp.float32) + lax.ppermute(theirs, "yhi", swap).astype(jnp.float32)
    ).astype(jnp.bfloat16)

    partial_value = lax.dot_general(
        hidden, gathered, (((1,), (1,)), ((), ())), preferred_element_type=jnp.float32
    ).astype(jnp.bfloat16)
    partial_value = partial_value.reshape(tokens_here, n_core, n_yhi, n_z, rows_w).transpose(
        0, 3, 2, 1, 4
    )
    partial_value = jnp.where(own_first, partial_value, jnp.flip(partial_value, axis=2)).reshape(
        tokens_here, n_tensor, d_all // n_tensor
    )
    layer_out = sum_to_bf16(lax.all_to_all(partial_value, "tensor", 1, 1, tiled=True), 1)
    hidden_grad = jnp.dot(weighted_p, gathered, preferred_element_type=jnp.float32).astype(
        jnp.bfloat16
    )
    return (layer_out, hidden_grad, weight_grad)


def solution(mesh):
    n_tensor = mesh.shape["tensor"]
    fine = Mesh(mesh.devices.reshape(-1, 2, 2, n_tensor), ("z", "yhi", "core", "tensor"))
    return jax.shard_map(
        shards,
        mesh=fine,
        in_specs=(
            P(SAMPLE, "tensor"),
            P(SAMPLE, "tensor"),
            P(SAMPLE, None),
            P(SAMPLE),
            P(SAMPLE),
        ),
        out_specs=(P(SAMPLE, "tensor"), P(SAMPLE, "tensor"), P(SAMPLE, "tensor")),
        check_vma=False,
    )
```

```python
import math

import jax
import jax.numpy as jnp
from jax import lax
from jax.sharding import Mesh
from jax.sharding import PartitionSpec as P

GROUP = 32
SAMPLE = ("z", "yhi", "core")


def sum_to_bf16(received, axis):
    return jnp.sum(received.astype(jnp.float32), axis=axis).astype(jnp.bfloat16)


def shards(hidden, down_weight, cotangent, scores, prompt_ids):
    samples_here = scores.shape[0]
    n_sample = lax.axis_size(SAMPLE)
    n_z = lax.axis_size("z")
    n_yhi = lax.axis_size("yhi")
    n_core = lax.axis_size("core")
    n_tensor = lax.axis_size("tensor")
    prompts = samples_here * n_sample // GROUP

    packed = jnp.concatenate([scores, prompt_ids])[None, :]
    everything = lax.all_gather(packed, SAMPLE, axis=0, tiled=True)
    all_scores = everything[:, :samples_here].reshape(-1)
    all_ids = everything[:, samples_here:].reshape(-1)
    all_rewards = all_scores.astype(jnp.float32) / 64.0
    all_onehot = all_ids[:, None] == jnp.arange(prompts, dtype=jnp.int32)[None, :]
    peak = jnp.max(jnp.where(all_onehot, all_rewards[:, None], jnp.float32(-1e30)), axis=0)
    shifted = jnp.where(all_onehot, jnp.exp(all_rewards[:, None] - peak[None, :]), 0.0)
    total = jnp.sum(shifted, axis=0)
    log_norm = peak + jnp.log(total)

    rewards = scores.astype(jnp.float32) / 64.0
    onehot = prompt_ids[:, None] == jnp.arange(prompts, dtype=jnp.int32)[None, :]
    sample_norm = jnp.sum(jnp.where(onehot, log_norm[None, :], 0.0), axis=1)
    tokens_here = hidden.shape[0]
    token_weight = jnp.repeat(GROUP * jnp.exp(rewards - sample_norm), tokens_here // samples_here)
    weighted = (cotangent.astype(jnp.float32) * token_weight[:, None]).astype(jnp.bfloat16)

    rows_w = down_weight.shape[0]
    d_all = weighted.shape[1]
    d_half = d_all // n_core
    own_first = lax.axis_index("yhi") == 0
    my_core = lax.axis_index("core")
    swap = [(0, 1), (1, 0)]
    weighted_5 = weighted.reshape(tokens_here, n_z, n_yhi, n_core, rows_w)
    weighted_rel = jnp.where(own_first, weighted_5, jnp.flip(weighted_5, axis=2))
    weighted_mine = lax.dynamic_index_in_dim(weighted_rel, my_core, axis=3, keepdims=False)
    weighted_mine = weighted_mine.reshape(tokens_here, d_half)
    weighted_theirs = lax.dynamic_index_in_dim(weighted_rel, 1 - my_core, axis=3, keepdims=False)
    weighted_recv = lax.ppermute(weighted_theirs.reshape(tokens_here, d_half), "core", swap)
    hidden_recv = lax.ppermute(hidden, "core", swap)

    gathered = jnp.concatenate([down_weight, lax.ppermute(down_weight, "yhi", swap)], axis=0)
    gathered = lax.all_gather(gathered, "z", axis=0, tiled=True)

    scale = 1.0 / math.sqrt(tokens_here * n_sample)
    grad_part = (
        lax.dot_general(
            jnp.concatenate([weighted_mine, weighted_recv], axis=0),
            jnp.concatenate([hidden, hidden_recv], axis=0),
            (((0,), (0,)), ((), ())),
            preferred_element_type=jnp.float32,
        )
        * scale
    ).astype(jnp.bfloat16)
    grad_part = lax.psum_scatter(grad_part, "z", scatter_dimension=0, tiled=True)
    weight_grad = (
        grad_part[:rows_w].astype(jnp.float32)
        + lax.ppermute(grad_part[rows_w:], "yhi", swap).astype(jnp.float32)
    ).astype(jnp.bfloat16)

    def value_of(rows):
        return lax.dot_general(
            rows, gathered, (((1,), (1,)), ((), ())), preferred_element_type=jnp.float32
        ).astype(jnp.bfloat16)

    value_mine = value_of(hidden)
    value_recv = lax.ppermute(value_of(hidden_recv), "core", swap)
    partial_value = jnp.stack([value_mine, value_recv], axis=1)
    partial_value = jnp.where(my_core == 0, partial_value, jnp.flip(partial_value, axis=1))
    partial_value = partial_value.reshape(tokens_here, n_core, n_z, n_yhi, rows_w).transpose(
        0, 2, 3, 1, 4
    )
    partial_value = jnp.where(own_first, partial_value, jnp.flip(partial_value, axis=2)).reshape(
        tokens_here, n_tensor, d_all // n_tensor
    )
    layer_out = sum_to_bf16(lax.all_to_all(partial_value, "tensor", 1, 1, tiled=True), 1)
    grad_for_other = jnp.dot(weighted_recv, gathered, preferred_element_type=jnp.float32)
    hidden_grad = (
        jnp.dot(weighted_mine, gathered, preferred_element_type=jnp.float32)
        + lax.ppermute(grad_for_other, "core", swap)
    ).astype(jnp.bfloat16)
    return (layer_out, hidden_grad, weight_grad)


def solution(mesh):
    n_tensor = mesh.shape["tensor"]
    fine = Mesh(mesh.devices.reshape(-1, 2, 2, n_tensor), ("z", "yhi", "core", "tensor"))
    return jax.shard_map(
        shards,
        mesh=fine,
        in_specs=(
            P(SAMPLE, "tensor"),
            P(SAMPLE, "tensor"),
            P(SAMPLE, None),
            P(SAMPLE),
            P(SAMPLE),
        ),
        out_specs=(P(SAMPLE, "tensor"), P(SAMPLE, "tensor"), P(SAMPLE, "tensor")),
        check_vma=False,
    )
```

```python
import math

import jax
import jax.numpy as jnp
from jax import lax
from jax.sharding import Mesh
from jax.sharding import PartitionSpec as P

GROUP = 32
SAMPLE = ("z", "yhi", "core")


def sum_to_bf16(received, axis):
    return jnp.sum(received.astype(jnp.float32), axis=axis).astype(jnp.bfloat16)


def shards(hidden, down_weight, cotangent, scores, prompt_ids):
    samples_here = scores.shape[0]
    n_sample = lax.axis_size(SAMPLE)
    n_z = lax.axis_size("z")
    n_yhi = lax.axis_size("yhi")
    n_core = lax.axis_size("core")
    n_tensor = lax.axis_size("tensor")
    prompts = samples_here * n_sample // GROUP

    packed = jnp.concatenate([scores, prompt_ids])[None, :]
    everything = lax.all_gather(packed, SAMPLE, axis=0, tiled=True)
    all_scores = everything[:, :samples_here].reshape(-1)
    all_ids = everything[:, samples_here:].reshape(-1)
    all_rewards = all_scores.astype(jnp.float32) / 64.0
    all_onehot = all_ids[:, None] == jnp.arange(prompts, dtype=jnp.int32)[None, :]
    peak = jnp.max(jnp.where(all_onehot, all_rewards[:, None], jnp.float32(-1e30)), axis=0)
    shifted = jnp.where(all_onehot, jnp.exp(all_rewards[:, None] - peak[None, :]), 0.0)
    total = jnp.sum(shifted, axis=0)
    log_norm = peak + jnp.log(total)

    rewards = scores.astype(jnp.float32) / 64.0
    onehot = prompt_ids[:, None] == jnp.arange(prompts, dtype=jnp.int32)[None, :]
    sample_norm = jnp.sum(jnp.where(onehot, log_norm[None, :], 0.0), axis=1)
    tokens_here = hidden.shape[0]
    token_weight = jnp.repeat(GROUP * jnp.exp(rewards - sample_norm), tokens_here // samples_here)
    weighted = (cotangent.astype(jnp.float32) * token_weight[:, None]).astype(jnp.bfloat16)

    rows_w = down_weight.shape[0]
    d_all = weighted.shape[1]
    d_half = d_all // n_core
    own_first = lax.axis_index("yhi") == 0
    my_core = lax.axis_index("core")
    swap = [(0, 1), (1, 0)]
    weighted_5 = weighted.reshape(tokens_here, n_z, n_yhi, n_core, rows_w)
    weighted_rel = jnp.where(own_first, weighted_5, jnp.flip(weighted_5, axis=2))
    weighted_mine = lax.dynamic_index_in_dim(weighted_rel, my_core, axis=3, keepdims=False)
    weighted_mine = weighted_mine.reshape(tokens_here, d_half)
    weighted_theirs = lax.dynamic_index_in_dim(weighted_rel, 1 - my_core, axis=3, keepdims=False)
    weighted_recv = lax.ppermute(weighted_theirs.reshape(tokens_here, d_half), "core", swap)
    hidden_recv = lax.ppermute(hidden, "core", swap)

    gathered = jnp.concatenate([down_weight, lax.ppermute(down_weight, "yhi", swap)], axis=0)
    gathered = lax.all_gather(gathered, "z", axis=0, tiled=True)

    scale = 1.0 / math.sqrt(tokens_here * n_sample)
    grad_part = (
        lax.dot_general(
            jnp.concatenate([weighted_mine, weighted_recv], axis=0),
            jnp.concatenate([hidden, hidden_recv], axis=0),
            (((0,), (0,)), ((), ())),
            preferred_element_type=jnp.float32,
        )
        * scale
    ).astype(jnp.bfloat16)
    grad_part = grad_part.reshape(n_z, -1, grad_part.shape[1])
    grad_part = jnp.sum(
        lax.all_to_all(grad_part, "z", 0, 0, tiled=True).astype(jnp.float32), axis=0
    )
    weight_grad = (
        grad_part[:rows_w]
        + lax.ppermute(grad_part[rows_w:].astype(jnp.bfloat16), "yhi", swap).astype(jnp.float32)
    ).astype(jnp.bfloat16)

    def value_of(rows):
        return lax.dot_general(
            rows, gathered, (((1,), (1,)), ((), ())), preferred_element_type=jnp.float32
        ).astype(jnp.bfloat16)

    value_mine = value_of(hidden)
    value_recv = lax.ppermute(value_of(hidden_recv), "core", swap)
    partial_value = jnp.stack([value_mine, value_recv], axis=1)
    partial_value = jnp.where(my_core == 0, partial_value, jnp.flip(partial_value, axis=1))
    partial_value = partial_value.reshape(tokens_here, n_core, n_z, n_yhi, rows_w).transpose(
        0, 2, 3, 1, 4
    )
    partial_value = jnp.where(own_first, partial_value, jnp.flip(partial_value, axis=2)).reshape(
        tokens_here, n_tensor, d_all // n_tensor
    )
    layer_out = sum_to_bf16(lax.all_to_all(partial_value, "tensor", 1, 1, tiled=True), 1)
    grad_for_other = jnp.dot(weighted_recv, gathered, preferred_element_type=jnp.float32)
    hidden_grad = (
        jnp.dot(weighted_mine, gathered, preferred_element_type=jnp.float32)
        + lax.ppermute(grad_for_other, "core", swap)
    ).astype(jnp.bfloat16)
    return (layer_out, hidden_grad, weight_grad)


def solution(mesh):
    n_tensor = mesh.shape["tensor"]
    fine = Mesh(mesh.devices.reshape(-1, 2, 2, n_tensor), ("z", "yhi", "core", "tensor"))
    return jax.shard_map(
        shards,
        mesh=fine,
        in_specs=(
            P(SAMPLE, "tensor"),
            P(SAMPLE, "tensor"),
            P(SAMPLE, None),
            P(SAMPLE),
            P(SAMPLE),
        ),
        out_specs=(P(SAMPLE, "tensor"), P(SAMPLE, "tensor"), P(SAMPLE, "tensor")),
        check_vma=False,
    )
```

```python
import math

import jax
import jax.numpy as jnp
from jax import lax
from jax.sharding import Mesh
from jax.sharding import PartitionSpec as P

GROUP = 32
SAMPLE = ("z", "yhi", "core")


def sum_to_bf16(received, axis):
    return jnp.sum(received.astype(jnp.float32), axis=axis).astype(jnp.bfloat16)


def shards(hidden, down_weight, cotangent, scores, prompt_ids):
    samples_here = scores.shape[0]
    n_sample = lax.axis_size(SAMPLE)
    n_z = lax.axis_size("z")
    n_yhi = lax.axis_size("yhi")
    n_core = lax.axis_size("core")
    n_tensor = lax.axis_size("tensor")
    prompts = samples_here * n_sample // GROUP

    packed = jnp.concatenate([scores, prompt_ids])[None, :]
    everything = lax.all_gather(packed, SAMPLE, axis=0, tiled=True)
    all_scores = everything[:, :samples_here].reshape(-1)
    all_ids = everything[:, samples_here:].reshape(-1)
    all_rewards = all_scores.astype(jnp.float32) / 64.0
    all_onehot = all_ids[:, None] == jnp.arange(prompts, dtype=jnp.int32)[None, :]
    peak = jnp.max(jnp.where(all_onehot, all_rewards[:, None], jnp.float32(-1e30)), axis=0)
    shifted = jnp.where(all_onehot, jnp.exp(all_rewards[:, None] - peak[None, :]), 0.0)
    total = jnp.sum(shifted, axis=0)
    log_norm = peak + jnp.log(total)

    rewards = scores.astype(jnp.float32) / 64.0
    onehot = prompt_ids[:, None] == jnp.arange(prompts, dtype=jnp.int32)[None, :]
    sample_norm = jnp.sum(jnp.where(onehot, log_norm[None, :], 0.0), axis=1)
    tokens_here = hidden.shape[0]
    token_weight = jnp.repeat(GROUP * jnp.exp(rewards - sample_norm), tokens_here // samples_here)
    weighted = (cotangent.astype(jnp.float32) * token_weight[:, None]).astype(jnp.bfloat16)

    rows_w = down_weight.shape[0]
    d_all = weighted.shape[1]
    d_half = d_all // n_core
    own_first = lax.axis_index("yhi") == 0
    my_core = lax.axis_index("core")
    swap = [(0, 1), (1, 0)]
    weighted_5 = weighted.reshape(tokens_here, n_z, n_yhi, n_core, rows_w)
    weighted_rel = jnp.where(own_first, weighted_5, jnp.flip(weighted_5, axis=2))
    weighted_mine = lax.dynamic_index_in_dim(weighted_rel, my_core, axis=3, keepdims=False)
    weighted_mine = weighted_mine.reshape(tokens_here, d_half)
    weighted_theirs = lax.dynamic_index_in_dim(weighted_rel, 1 - my_core, axis=3, keepdims=False)
    weighted_recv = lax.ppermute(weighted_theirs.reshape(tokens_here, d_half), "core", swap)
    hidden_recv = lax.ppermute(hidden, "core", swap)

    gathered = jnp.concatenate([down_weight, lax.ppermute(down_weight, "yhi", swap)], axis=0)
    gathered = lax.all_gather(gathered, "z", axis=0, tiled=True)

    scale = 1.0 / math.sqrt(tokens_here * n_sample)
    yhi_major = jnp.concatenate([weighted_mine, weighted_recv], axis=0)
    yhi_major = (
        yhi_major.reshape(-1, n_z, n_yhi, rows_w).transpose(0, 2, 1, 3).reshape(-1, d_half)
    )
    grad_part = (
        lax.dot_general(
            yhi_major,
            jnp.concatenate([hidden, hidden_recv], axis=0),
            (((0,), (0,)), ((), ())),
            preferred_element_type=jnp.float32,
        )
        * scale
    ).astype(jnp.bfloat16)
    half = grad_part.shape[0] // n_yhi
    grad_part = (
        grad_part[:half].astype(jnp.float32)
        + lax.ppermute(grad_part[half:], "yhi", swap).astype(jnp.float32)
    ).astype(jnp.bfloat16)
    weight_grad = lax.psum_scatter(grad_part, "z", scatter_dimension=0, tiled=True)

    def value_of(rows):
        return lax.dot_general(
            rows, gathered, (((1,), (1,)), ((), ())), preferred_element_type=jnp.float32
        ).astype(jnp.bfloat16)

    value_mine = value_of(hidden)
    value_recv = lax.ppermute(value_of(hidden_recv), "core", swap)
    partial_value = jnp.stack([value_mine, value_recv], axis=1)
    partial_value = jnp.where(my_core == 0, partial_value, jnp.flip(partial_value, axis=1))
    partial_value = partial_value.reshape(tokens_here, n_core, n_z, n_yhi, rows_w).transpose(
        0, 2, 3, 1, 4
    )
    partial_value = jnp.where(own_first, partial_value, jnp.flip(partial_value, axis=2)).reshape(
        tokens_here, n_tensor, d_all // n_tensor
    )
    layer_out = sum_to_bf16(lax.all_to_all(partial_value, "tensor", 1, 1, tiled=True), 1)
    grad_for_other = jnp.dot(weighted_recv, gathered, preferred_element_type=jnp.float32)
    hidden_grad = (
        jnp.dot(weighted_mine, gathered, preferred_element_type=jnp.float32)
        + lax.ppermute(grad_for_other, "core", swap)
    ).astype(jnp.bfloat16)
    return (layer_out, hidden_grad, weight_grad)


def solution(mesh):
    n_tensor = mesh.shape["tensor"]
    fine = Mesh(mesh.devices.reshape(-1, 2, 2, n_tensor), ("z", "yhi", "core", "tensor"))
    return jax.shard_map(
        shards,
        mesh=fine,
        in_specs=(
            P(SAMPLE, "tensor"),
            P(SAMPLE, "tensor"),
            P(SAMPLE, None),
            P(SAMPLE),
            P(SAMPLE),
        ),
        out_specs=(P(SAMPLE, "tensor"), P(SAMPLE, "tensor"), P(SAMPLE, "tensor")),
        check_vma=False,
    )
```
